1024 devices in a mesh: seq: 64 (over z, x_hi), fsdp: 16 (over x_lo, y, core).
Axes of the slice: x: 4 (x_hi: 2, x_lo: 2; x = x_hi * 2 + x_lo), y: 4, z: 32, core: 2. Of those that a mesh axis runs over, the one named last changes fastest.
Arguments:
- projected: bfloat16 [3, 8192, 32768], P(None, 'fsdp', 'seq'), may hold values from -6 to 6
- short_weight: float32 [3, 8192, 3], P(None, 'fsdp'), may hold values from -3.5 to 3.5
- skip_weight: float32 [8192], P('fsdp'), may hold values from -4 to 4
- decay_rates: float32 [8192, 16], P('fsdp'), may hold values from 1.5258789e-05 to 0.05
- residues: float32 [8192, 16], P('fsdp'), may hold values from -1.5 to 1.5
Outputs:
- output: bfloat16 [8192, 32768], P('fsdp', 'seq')
The draws below stay inside these ranges and needn't reach their ends.
All inputs are finite; a program needn't handle non-finite values.
Results may differ from the reference program's by a relative error of at most 0.0058.
Values may be sent and summed in bfloat16 or wider, within the bound.
No kernel may reach another device: no remote copies, remote signals or barrier semaphores. Data moves between devices by JAX's collectives and lax.ppermute only.
A program may use at most 64 MiB of HBM per device.

```python
import math
import jax
import jax.numpy as jnp
from jax import lax

D = 8192
ORDER = 16
KS = 3
TOKENS = 32768


def shard_levels(key, dims, pieces, low, high):
    def one(dim, shards_of):
        heights = jax.random.uniform(jax.random.fold_in(jax.random.fold_in(key, 6), dim), (shards_of,), jnp.float32, low / len(pieces), high / len(pieces))
        return jnp.repeat(jnp.exp(heights), dims[dim] // shards_of).reshape((-1,) + (1,) * (len(dims) - dim - 1))

    loudness = one(*pieces[0])
    for cut in pieces[1:]:
        loudness = loudness * one(*cut)
    return loudness


def noise(own_key, shape, deviation, most, cuts=(), kind=jnp.bfloat16):
    entries = jax.random.normal(own_key, shape, jnp.float32) * deviation
    if len(cuts) > 0:
        entries = shard_levels(own_key, shape, cuts, -0.22, 0.18) * entries
    return jnp.clip(entries, min=-most, max=most).astype(kind)


def setup_inputs(seed: int = 0) -> dict:
    seeds = jax.random.split(jax.random.key(seed), 6)
    return {
        "projected": noise(seeds[0], (3, D, TOKENS), 1.0, 6.0, ((1, 16), (2, 64))),
        "short_weight": noise(seeds[1], (3, D, KS), KS ** -0.5, 3.5, ((1, 16),), jnp.float32),
        "skip_weight": noise(seeds[2], (D,), 1.0, 4.0, ((0, 16),), jnp.float32),
        "decay_rates": jnp.clip(jnp.exp(math.log(0.05) - 8.094623 * jax.random.uniform(seeds[3], (D, ORDER), jnp.float32) ** shard_levels(seeds[3], (D, ORDER), ((0, 16),), -0.2, 0.2)), 1.52587890625e-05, 0.05),
        "residues": noise(seeds[4], (D, ORDER), 0.25, 1.5, ((0, 16),), jnp.float32),
    }


def reference(projected, short_weight, skip_weight, decay_rates, residues):
    length = projected.shape[2]
    taps_count = short_weight.shape[2]
    group = math.gcd(D, 32)

    def one_group(number):
        first = (number * group).astype(jnp.int32)
        block = lax.dynamic_slice_in_dim(projected, first, group, 1).astype(jnp.float32)
        weights = lax.dynamic_slice_in_dim(short_weight, first, group, 1)
        padded = jnp.pad(block, ((0, 0), (0, 0), (taps_count - 1, 0)))
        feats = jnp.zeros_like(block)
        for lag in range(taps_count):
            begin = taps_count - 1 - lag
            feats = feats + weights[:, :, lag][:, :, None] * padded[:, :, begin:begin + length]
        mixed = (feats[1] * feats[2]).astype(jnp.bfloat16)
        mixed = lax.optimization_barrier(mixed)
        signal = mixed.astype(jnp.float32)
        decay_rate = lax.dynamic_slice_in_dim(decay_rates, first, group, 0)
        residue = lax.dynamic_slice_in_dim(residues, first, group, 0)
        offsets = jnp.arange(length, dtype=jnp.float32)
        scaled = residue * jnp.sqrt(2.0 * decay_rate)
        filt = lax.optimization_barrier(jnp.sum(scaled[:, :, None] * jnp.exp(-decay_rate[:, :, None] * offsets), axis=1))
        padded_len = 2 * length
        spectrum = jnp.fft.rfft(filt, padded_len) * jnp.fft.rfft(signal, padded_len)
        convolved = jnp.fft.irfft(spectrum, padded_len)[:, :length]
        gains = lax.dynamic_slice_in_dim(skip_weight, first, group, 0)
        summed = (convolved + gains[:, None] * signal).astype(jnp.bfloat16)
        summed = lax.optimization_barrier(summed)
        return (feats[0] * summed.astype(jnp.float32)).astype(jnp.bfloat16)
    result = lax.map(one_group, jnp.arange(D // group, dtype=jnp.int32))
    return result.reshape(D, length)
```

```python
import jax
import jax.numpy as jnp
from jax import lax
from jax.sharding import PartitionSpec as P


def from_behind(value, axis, steps):
    count = lax.axis_size(axis)
    leading, last = (max(0, -steps), min(count, count - steps))
    return lax.ppermute(value, axis, [(source, source + steps) for source in range(leading, last)])


def short_conv(projected, short_weight):
    taps_count = short_weight.shape[2]
    length = projected.shape[2]
    tail = jnp.swapaxes(projected[:, :, length - (taps_count - 1) :], 1, 2)
    before = from_behind(tail, "seq", 1)
    padded = jnp.concatenate([jnp.swapaxes(before, 1, 2), projected], axis=2).astype(jnp.float32)
    feats = jnp.zeros(projected.shape, jnp.float32)
    for lag in range(taps_count):
        begin = taps_count - 1 - lag
        feats = feats + short_weight[:, :, lag][:, :, None] * padded[:, :, begin : begin + length]
    return feats


def shards(projected, short_weight, skip_weight, decay_rates, residues):
    channels = projected.shape[1]
    length = projected.shape[2]
    modes = decay_rates.shape[1]
    feats = short_conv(projected, short_weight)
    mixed = (feats[1] * feats[2]).astype(jnp.bfloat16)
    signal = mixed.astype(jnp.float32)

    block = min(128, length)
    count = length // block
    rate = decay_rates
    weight = residues * jnp.sqrt(2.0 * rate)
    offsets = jnp.arange(block, dtype=jnp.float32)
    rising = jnp.exp(rate[:, :, None] * offsets)
    falling = weight[:, :, None] * jnp.exp(-rate[:, :, None] * offsets)

    blocks = signal.reshape(channels, 1, count, block)
    scaled = blocks * rising[:, :, None, :]
    high = scaled.astype(jnp.bfloat16)
    low = (scaled - high.astype(jnp.float32)).astype(jnp.bfloat16)
    rows = jnp.arange(block)
    ones = (rows[:, None] <= rows[None, :]).astype(jnp.bfloat16)
    pair = jnp.concatenate([high, low], axis=3)
    stacked = jnp.concatenate([ones, ones], axis=0)
    running = jnp.einsum("ckni,ij->cknj", pair, stacked, preferred_element_type=jnp.float32)

    block_sums = jnp.sum(scaled, axis=3) * jnp.exp(-rate * (block - 1))[:, :, None]
    step = jnp.exp(-rate * block)
    carried = [jnp.zeros_like(rate)]
    for n in range(count):
        carried.append(step * carried[-1] + block_sums[:, :, n])
    local_final = carried[-1]
    local_states = jnp.stack(carried[:count], axis=2)

    gathered = lax.all_gather(local_final, "seq")
    devices = gathered.shape[0]
    here = lax.axis_index("seq")
    others = jnp.arange(devices)
    distance = here - 1 - others
    decay_between = jnp.exp(
        -rate[None, :, :] * (length * jnp.maximum(distance, 0)).astype(jnp.float32)[:, None, None]
    )
    decay_between = jnp.where((others < here)[:, None, None], decay_between, 0.0)
    incoming = jnp.sum(decay_between * gathered, axis=0)

    starts = (jnp.arange(count) * block + 1).astype(jnp.float32)
    entering = jnp.exp(-rate)[:, :, None] * local_states + jnp.exp(-rate[:, :, None] * starts) * incoming[:, :, None]
    convolved = jnp.sum(falling[:, :, None, :] * (running + entering[:, :, :, None]), axis=1)
    convolved = convolved.reshape(channels, length)
    summed = (convolved + skip_weight[:, None] * signal).astype(jnp.bfloat16)
    return (feats[0] * summed.astype(jnp.float32)).astype(jnp.bfloat16)


def solution(mesh):
    return jax.shard_map(
        shards,
        mesh=mesh,
        in_specs=(
            P(None, "fsdp", "seq"),
            P(None, "fsdp", None),
            P("fsdp"),
            P("fsdp", None),
            P("fsdp", None),
        ),
        out_specs=P("fsdp", "seq"),
        check_vma=False,
    )
```

```python
import jax
import jax.numpy as jnp
from jax import lax
from jax.sharding import PartitionSpec as P


def from_behind(value, axis, steps):
    count = lax.axis_size(axis)
    leading, last = (max(0, -steps), min(count, count - steps))
    return lax.ppermute(value, axis, [(source, source + steps) for source in range(leading, last)])


def short_conv(projected, short_weight):
    taps_count = short_weight.shape[2]
    length = projected.shape[2]
    tail = jnp.swapaxes(projected[:, :, length - (taps_count - 1) :], 1, 2)
    before = from_behind(tail, "seq", 1)
    padded = jnp.concatenate([jnp.swapaxes(before, 1, 2), projected], axis=2).astype(jnp.float32)
    feats = jnp.zeros(projected.shape, jnp.float32)
    for lag in range(taps_count):
        begin = taps_count - 1 - lag
        feats = feats + short_weight[:, :, lag][:, :, None] * padded[:, :, begin : begin + length]
    return feats


def scan_states(final, rate, length):
    count = lax.axis_size("seq")
    acc = from_behind(final, "seq", 1)
    if count > 2:
        acc = acc + jnp.exp(-rate * length) * from_behind(final, "seq", 2)
    shift = 2
    while shift < count:
        acc = acc + jnp.exp(-rate * float(length * shift)) * from_behind(acc, "seq", shift)
        shift *= 2
    return acc


def shards(projected, short_weight, skip_weight, decay_rates, residues):
    channels = projected.shape[1]
    length = projected.shape[2]
    modes = decay_rates.shape[1]
    feats = short_conv(projected, short_weight)
    mixed = (feats[1] * feats[2]).astype(jnp.bfloat16)
    signal = mixed.astype(jnp.float32)

    block = min(128, length)
    count = length // block
    rate = decay_rates
    weight = residues * jnp.sqrt(2.0 * rate)
    offsets = jnp.arange(block, dtype=jnp.float32)
    rising = jnp.exp(rate[:, :, None] * offsets)
    falling = weight[:, :, None] * jnp.exp(-rate[:, :, None] * offsets)

    blocks = signal.reshape(channels, 1, count, block)
    scaled = blocks * rising[:, :, None, :]
    high = scaled.astype(jnp.bfloat16)
    low = (scaled - high.astype(jnp.float32)).astype(jnp.bfloat16)
    rows = jnp.arange(block)
    ones = (rows[:, None] <= rows[None, :]).astype(jnp.bfloat16)
    pair = jnp.concatenate([high, low], axis=3)
    stacked = jnp.concatenate([ones, ones], axis=0)
    running = jnp.einsum("ckni,ij->cknj", pair, stacked, preferred_element_type=jnp.float32)

    block_sums = jnp.sum(scaled, axis=3) * jnp.exp(-rate * (block - 1))[:, :, None]
    step = jnp.exp(-rate * block)
    carried = [jnp.zeros_like(rate)]
    for n in range(count):
        carried.append(step * carried[-1] + block_sums[:, :, n])
    local_final = carried[-1]
    local_states = jnp.stack(carried[:count], axis=2)

    incoming = scan_states(local_final, rate, length)

    local_part = jnp.exp(-rate)[:, :, None] * local_states
    convolved = jnp.sum(falling[:, :, None, :] * (running + local_part[:, :, :, None]), axis=1)
    starts = (jnp.arange(count) * block + 1).astype(jnp.float32)
    entering = jnp.exp(-rate[:, :, None] * starts) * incoming[:, :, None]
    convolved = convolved + jnp.sum(falling[:, :, None, :] * entering[:, :, :, None], axis=1)
    convolved = convolved.reshape(channels, length)
    summed = (convolved + skip_weight[:, None] * signal).astype(jnp.bfloat16)
    return (feats[0] * summed.astype(jnp.float32)).astype(jnp.bfloat16)


def solution(mesh):
    return jax.shard_map(
        shards,
        mesh=mesh,
        in_specs=(
            P(None, "fsdp", "seq"),
            P(None, "fsdp", None),
            P("fsdp"),
            P("fsdp", None),
            P("fsdp", None),
        ),
        out_specs=P("fsdp", "seq"),
        check_vma=False,
    )
```

```python
import jax
import jax.numpy as jnp
from jax import lax
from jax.sharding import PartitionSpec as P


def from_behind(value, axis, steps):
    count = lax.axis_size(axis)
    leading, last = (max(0, -steps), min(count, count - steps))
    return lax.ppermute(value, axis, [(source, source + steps) for source in range(leading, last)])


def short_conv(projected, short_weight):
    taps_count = short_weight.shape[2]
    length = projected.shape[2]
    tail = jnp.swapaxes(projected[:, :, length - (taps_count - 1) :], 1, 2)
    before = from_behind(tail, "seq", 1)
    padded = jnp.concatenate([jnp.swapaxes(before, 1, 2), projected], axis=2).astype(jnp.float32)
    feats = jnp.zeros(projected.shape, jnp.float32)
    for lag in range(taps_count):
        begin = taps_count - 1 - lag
        feats = feats + short_weight[:, :, lag][:, :, None] * padded[:, :, begin : begin + length]
    return feats


def moved(value, pairs):
    return lax.ppermute(value, "seq", pairs)


def scan_states(final, rate, length):
    count = lax.axis_size("seq")
    ring = count // 2
    half = ring // 2
    here = lax.axis_index("seq")
    z = here // 2
    odd = here % 2
    unit = jnp.exp(-rate * float(length))
    partner = moved(final, [(d, d ^ 1) for d in range(count)])
    first = jnp.where(odd == 1, partner, final)
    second = jnp.where(odd == 1, final, partner)
    pair = unit * first + second

    def forward(value, steps):
        pairs = [(d, d + 2 * steps) for d in range(count) if d + 2 * steps < count]
        return moved(value, pairs) if pairs else jnp.zeros_like(value)

    def backward(value, steps):
        return moved(value, [(d, (d - 2 * steps) % count) for d in range(count)])

    def decay(steps):
        return jnp.exp(-rate * float(2 * length * steps))

    near = forward(pair, 1) + decay(1) * forward(pair, 2)
    far = jnp.where(z < half, pair, 0.0)
    width = 1
    while width < half:
        near = near + decay(width * 2) * forward(near, width * 2) if width * 2 < half else near
        far = decay(width) * far + backward(far, width)
        width *= 2
    near_done = near
    whole = near_done + jnp.where(z > half, decay(half), 0.0) * far
    return jnp.where(odd == 1, unit * whole + first, whole)


def shards(projected, short_weight, skip_weight, decay_rates, residues):
    channels = projected.shape[1]
    length = projected.shape[2]
    modes = decay_rates.shape[1]
    feats = short_conv(projected, short_weight)
    mixed = (feats[1] * feats[2]).astype(jnp.bfloat16)
    signal = mixed.astype(jnp.float32)

    block = min(128, length)
    count = length // block
    rate = decay_rates
    weight = residues * jnp.sqrt(2.0 * rate)
    offsets = jnp.arange(block, dtype=jnp.float32)
    rising = jnp.exp(rate[:, :, None] * offsets)
    falling = weight[:, :, None] * jnp.exp(-rate[:, :, None] * offsets)

    blocks = signal.reshape(channels, 1, count, block)
    scaled = blocks * rising[:, :, None, :]
    high = scaled.astype(jnp.bfloat16)
    low = (scaled - high.astype(jnp.float32)).astype(jnp.bfloat16)
    rows = jnp.arange(block)
    ones = (rows[:, None] <= rows[None, :]).astype(jnp.bfloat16)
    pair = jnp.concatenate([high, low], axis=3)
    stacked = jnp.concatenate([ones, ones], axis=0)
    running = jnp.einsum("ckni,ij->cknj", pair, stacked, preferred_element_type=jnp.float32)

    block_sums = jnp.sum(scaled, axis=3) * jnp.exp(-rate * (block - 1))[:, :, None]
    step = jnp.exp(-rate * block)
    carried = [jnp.zeros_like(rate)]
    for n in range(count):
        carried.append(step * carried[-1] + block_sums[:, :, n])
    local_final = carried[-1]
    local_states = jnp.stack(carried[:count], axis=2)

    incoming = scan_states(local_final, rate, length)

    local_part = jnp.exp(-rate)[:, :, None] * local_states
    convolved = jnp.sum(falling[:, :, None, :] * (running + local_part[:, :, :, None]), axis=1)
    starts = (jnp.arange(count) * block + 1).astype(jnp.float32)
    entering = jnp.exp(-rate[:, :, None] * starts) * incoming[:, :, None]
    convolved = convolved + jnp.sum(falling[:, :, None, :] * entering[:, :, :, None], axis=1)
    convolved = convolved.reshape(channels, length)
    summed = (convolved + skip_weight[:, None] * signal).astype(jnp.bfloat16)
    return (feats[0] * summed.astype(jnp.float32)).astype(jnp.bfloat16)


def solution(mesh):
    return jax.shard_map(
        shards,
        mesh=mesh,
        in_specs=(
            P(None, "fsdp", "seq"),
            P(None, "fsdp", None),
            P("fsdp"),
            P("fsdp", None),
            P("fsdp", None),
        ),
        out_specs=P("fsdp", "seq"),
        check_vma=False,
    )
```

```python
import jax
import jax.numpy as jnp
from jax import lax
from jax.sharding import PartitionSpec as P


def from_behind(value, axis, steps):
    count = lax.axis_size(axis)
    leading, last = (max(0, -steps), min(count, count - steps))
    return lax.ppermute(value, axis, [(source, source + steps) for source in range(leading, last)])


def short_conv(projected, short_weight):
    taps_count = short_weight.shape[2]
    length = projected.shape[2]
    tail = jnp.swapaxes(projected[:, :, length - (taps_count - 1) :], 1, 2)
    before = from_behind(tail, "seq", 1)
    padded = jnp.concatenate([jnp.swapaxes(before, 1, 2), projected], axis=2).astype(jnp.float32)
    feats = jnp.zeros(projected.shape, jnp.float32)
    for lag in range(taps_count):
        begin = taps_count - 1 - lag
        feats = feats + short_weight[:, :, lag][:, :, None] * padded[:, :, begin : begin + length]
    return feats


def scan_states(final, rate, length):
    count = lax.axis_size("seq")

    def earlier(value, steps):
        pairs = [(d, d + steps) for d in range(count) if d + steps < count]
        return lax.ppermute(value, "seq", pairs) if pairs else jnp.zeros_like(value)

    def decay(steps):
        return jnp.exp(-rate * float(length * steps))

    width = min(4, count)
    acc = earlier(final, 1)
    for lag in range(2, width + 1):
        acc = acc + decay(lag - 1) * earlier(final, lag)
    while width < count:
        parts = [acc]
        for piece in range(1, 4):
            if piece * width < count:
                parts.append(decay(piece * width) * earlier(acc, piece * width))
        acc = sum(parts[1:], parts[0])
        width *= 4
    return acc


def shards(projected, short_weight, skip_weight, decay_rates, residues):
    channels = projected.shape[1]
    length = projected.shape[2]
    feats = short_conv(projected, short_weight)
    mixed = (feats[1] * feats[2]).astype(jnp.bfloat16)
    signal = mixed.astype(jnp.float32)

    block = min(128, length)
    count = length // block
    rate = decay_rates.T
    weight = (residues * jnp.sqrt(2.0 * decay_rates)).T
    offsets = jnp.arange(block, dtype=jnp.float32)
    rising = jnp.exp(rate[:, :, None] * offsets)
    falling = weight[:, :, None] * jnp.exp(-rate[:, :, None] * offsets)

    blocks = signal.reshape(1, channels, count, block)
    scaled = blocks * rising[:, :, None, :]
    high = scaled.astype(jnp.bfloat16)
    low = (scaled - high.astype(jnp.float32)).astype(jnp.bfloat16)
    rows = jnp.arange(block)
    ones = (rows[:, None] <= rows[None, :]).astype(jnp.bfloat16)
    pair = jnp.concatenate([high, low], axis=3)
    stacked = jnp.concatenate([ones, ones], axis=0)
    running = jnp.einsum("kcni,ij->kcnj", pair, stacked, preferred_element_type=jnp.float32)

    block_sums = jnp.sum(scaled, axis=3) * jnp.exp(-rate * (block - 1))[:, :, None]
    step = jnp.exp(-rate * block)
    carried = [jnp.zeros_like(rate)]
    for n in range(count):
        carried.append(step * carried[-1] + block_sums[:, :, n])
    local_final = carried[-1]
    local_states = jnp.stack(carried[:count], axis=2)

    incoming = scan_states(local_final, rate, length)

    local_part = jnp.exp(-rate)[:, :, None] * local_states
    convolved = jnp.sum(falling[:, :, None, :] * (running + local_part[:, :, :, None]), axis=0)
    starts = (jnp.arange(count) * block + 1).astype(jnp.float32)
    entering = jnp.exp(-rate[:, :, None] * starts) * incoming[:, :, None]
    convolved = convolved + jnp.sum(falling[:, :, None, :] * entering[:, :, :, None], axis=0)
    convolved = convolved.reshape(channels, length)
    summed = (convolved + skip_weight[:, None] * signal).astype(jnp.bfloat16)
    return (feats[0] * summed.astype(jnp.float32)).astype(jnp.bfloat16)


def solution(mesh):
    return jax.shard_map(
        shards,
        mesh=mesh,
        in_specs=(
            P(None, "fsdp", "seq"),
            P(None, "fsdp", None),
            P("fsdp"),
            P("fsdp", None),
            P("fsdp", None),
        ),
        out_specs=P("fsdp", "seq"),
        check_vma=False,
    )
```

```python
import jax
import jax.numpy as jnp
from jax import lax
from jax.experimental import pallas as pl
from jax.sharding import PartitionSpec as P


def from_behind(value, axis, steps):
    count = lax.axis_size(axis)
    leading, last = (max(0, -steps), min(count, count - steps))
    return lax.ppermute(value, axis, [(source, source + steps) for source in range(leading, last)])


def short_conv(projected, short_weight):
    taps_count = short_weight.shape[2]
    length = projected.shape[2]
    tail = jnp.swapaxes(projected[:, :, length - (taps_count - 1) :], 1, 2)
    before = from_behind(tail, "seq", 1)
    padded = jnp.concatenate([jnp.swapaxes(before, 1, 2), projected], axis=2).astype(jnp.float32)
    feats = jnp.zeros(projected.shape, jnp.float32)
    for lag in range(taps_count):
        begin = taps_count - 1 - lag
        feats = feats + short_weight[:, :, lag][:, :, None] * padded[:, :, begin : begin + length]
    return feats


def scan_states(final, rate, length):
    count = lax.axis_size("seq")

    def earlier(value, steps):
        pairs = [(d, d + steps) for d in range(count) if d + steps < count]
        return lax.ppermute(value, "seq", pairs) if pairs else jnp.zeros_like(value)

    def decay(steps):
        return jnp.exp(-rate * float(length * steps))

    width = min(4, count)
    acc = earlier(final, 1)
    for lag in range(2, width + 1):
        acc = acc + decay(lag - 1) * earlier(final, lag)
    while width < count:
        parts = [acc]
        for piece in range(1, 4):
            if piece * width < count:
                parts.append(decay(piece * width) * earlier(acc, piece * width))
        acc = sum(parts[1:], parts[0])
        width *= 4
    return acc


def modal_kernel(x_ref, rate_ref, weight_ref, step_ref, end_ref, span_ref, out_ref, final_ref):
    channels, length = x_ref.shape
    modes = rate_ref.shape[1]
    block = 128
    count = length // block
    x = x_ref[...]
    lanes = lax.broadcasted_iota(jnp.int32, (channels, block), 1).astype(jnp.float32)
    rows = lax.broadcasted_iota(jnp.int32, (block, block), 0)
    cols = lax.broadcasted_iota(jnp.int32, (block, block), 1)
    ones = jnp.where(rows <= cols, 1.0, 0.0).astype(jnp.bfloat16)
    pieces = [x[:, n * block : (n + 1) * block] for n in range(count)]
    sums = [jnp.zeros((channels, block), jnp.float32) for n in range(count)]
    for k in range(modes):
        rate = rate_ref[:, k : k + 1]
        rising = jnp.exp(rate * lanes)
        falling = weight_ref[:, k : k + 1] * jnp.exp(-rate * lanes)
        scaled = jnp.concatenate([piece * rising for piece in pieces], axis=0)
        high = scaled.astype(jnp.bfloat16)
        low = (scaled - high.astype(jnp.float32)).astype(jnp.bfloat16)
        running = jnp.dot(high, ones, preferred_element_type=jnp.float32) + jnp.dot(
            low, ones, preferred_element_type=jnp.float32
        )
        state = jnp.zeros((channels, 1), jnp.float32)
        for n in range(count):
            part = running[n * channels : (n + 1) * channels]
            sums[n] = sums[n] + falling * (part + step_ref[:, k : k + 1] * state)
            state = span_ref[:, k : k + 1] * state + end_ref[:, k : k + 1] * part[:, block - 1 : block]
        final_ref[k] = state
    for n in range(count):
        out_ref[:, n * block : (n + 1) * block] = sums[n]


def local_modal(signal, rate, weight):
    channels, length = signal.shape
    modes = rate.shape[1]
    tile = min(64, channels)
    step = jnp.exp(-rate)
    end = jnp.exp(-rate * 127.0)
    span = jnp.exp(-rate * 128.0)
    rows = pl.BlockSpec((tile, length), lambda i: (i, 0))
    small = pl.BlockSpec((tile, modes), lambda i: (i, 0))
    return pl.pallas_call(
        modal_kernel,
        grid=(channels // tile,),
        in_specs=[rows, small, small, small, small, small],
        out_specs=[rows, pl.BlockSpec((modes, tile, 1), lambda i: (0, i, 0))],
        out_shape=[
            jax.ShapeDtypeStruct((channels, length), jnp.float32),
            jax.ShapeDtypeStruct((modes, channels, 1), jnp.float32),
        ],
    )(signal, rate, weight, step, end, span)


def shards(projected, short_weight, skip_weight, decay_rates, residues):
    channels = projected.shape[1]
    length = projected.shape[2]
    feats = short_conv(projected, short_weight)
    mixed = (feats[1] * feats[2]).astype(jnp.bfloat16)
    signal = mixed.astype(jnp.float32)
    weight = residues * jnp.sqrt(2.0 * decay_rates)
    convolved, local_final = local_modal(signal, decay_rates, weight)

    rate = decay_rates.T
    incoming = scan_states(local_final[:, :, 0], rate, length)
    offsets = jnp.arange(1, length + 1, dtype=jnp.float32)
    entering = jnp.sum((weight.T * incoming)[:, :, None] * jnp.exp(-rate[:, :, None] * offsets), axis=0)
    summed = (convolved + entering + skip_weight[:, None] * signal).astype(jnp.bfloat16)
    return (feats[0] * summed.astype(jnp.float32)).astype(jnp.bfloat16)


def solution(mesh):
    return jax.shard_map(
        shards,
        mesh=mesh,
        in_specs=(
            P(None, "fsdp", "seq"),
            P(None, "fsdp", None),
            P("fsdp"),
            P("fsdp", None),
            P("fsdp", None),
        ),
        out_specs=P("fsdp", "seq"),
        check_vma=False,
    )
```

```python
import jax
import jax.numpy as jnp
from jax import lax
from jax.experimental import pallas as pl
from jax.sharding import PartitionSpec as P


def from_behind(value, axis, steps):
    count = lax.axis_size(axis)
    leading, last = (max(0, -steps), min(count, count - steps))
    return lax.ppermute(value, axis, [(source, source + steps) for source in range(leading, last)])


def short_conv(projected, short_weight):
    taps_count = short_weight.shape[2]
    length = projected.shape[2]
    tail = jnp.swapaxes(projected[:, :, length - (taps_count - 1) :], 1, 2)
    before = from_behind(tail, "seq", 1)
    padded = jnp.concatenate([jnp.swapaxes(before, 1, 2), projected], axis=2).astype(jnp.float32)
    feats = jnp.zeros(projected.shape, jnp.float32)
    for lag in range(taps_count):
        begin = taps_count - 1 - lag
        feats = feats + short_weight[:, :, lag][:, :, None] * padded[:, :, begin : begin + length]
    return feats


def scan_states(final, rate, length):
    count = lax.axis_size("seq")

    def earlier(value, steps):
        pairs = [(d, d + steps) for d in range(count) if d + steps < count]
        return lax.ppermute(value, "seq", pairs) if pairs else jnp.zeros_like(value)

    def decay(steps):
        return jnp.exp(-rate * float(length * steps))

    width = min(4, count)
    acc = earlier(final, 1)
    for lag in range(2, width + 1):
        acc = acc + decay(lag - 1) * earlier(final, lag)
    while width < count:
        parts = [acc]
        for piece in range(1, 4):
            if piece * width < count:
                parts.append(decay(piece * width) * earlier(acc, piece * width))
        acc = sum(parts[1:], parts[0])
        width *= 4
    return acc


def modal_kernel(x_ref, rate_ref, weight_ref, step_ref, end_ref, span_ref, out_ref, final_ref):
    channels, length = x_ref.shape
    modes = rate_ref.shape[1]
    block = 128
    count = length // block
    x = x_ref[...]
    lanes = lax.broadcasted_iota(jnp.int32, (channels, block), 1).astype(jnp.float32)
    rows = lax.broadcasted_iota(jnp.int32, (block, block), 0)
    cols = lax.broadcasted_iota(jnp.int32, (block, block), 1)
    ones = jnp.where(rows <= cols, 1.0, 0.0).astype(jnp.bfloat16)
    pieces = [x[:, n * block : (n + 1) * block] for n in range(count)]
    scaled = jnp.concatenate(
        [piece * jnp.exp(rate_ref[:, k : k + 1] * lanes) for k in range(modes) for piece in pieces], axis=0
    )
    high = scaled.astype(jnp.bfloat16)
    low = (scaled - high.astype(jnp.float32)).astype(jnp.bfloat16)
    running = jnp.dot(high, ones, preferred_element_type=jnp.float32) + jnp.dot(
        low, ones, preferred_element_type=jnp.float32
    )
    sums = [jnp.zeros((channels, block), jnp.float32) for n in range(count)]
    for k in range(modes):
        falling = weight_ref[:, k : k + 1] * jnp.exp(-rate_ref[:, k : k + 1] * lanes)
        state = jnp.zeros((channels, 1), jnp.float32)
        for n in range(count):
            first = (k * count + n) * channels
            part = running[first : first + channels]
            sums[n] = sums[n] + falling * (part + step_ref[:, k : k + 1] * state)
            state = span_ref[:, k : k + 1] * state + end_ref[:, k : k + 1] * part[:, block - 1 : block]
        final_ref[k] = state
    for n in range(count):
        out_ref[:, n * block : (n + 1) * block] = sums[n]


def local_modal(signal, rate, weight):
    channels, length = signal.shape
    modes = rate.shape[1]
    tile = min(64, channels)
    step = jnp.exp(-rate)
    end = jnp.exp(-rate * 127.0)
    span = jnp.exp(-rate * 128.0)
    rows = pl.BlockSpec((tile, length), lambda i: (i, 0))
    small = pl.BlockSpec((tile, modes), lambda i: (i, 0))
    return pl.pallas_call(
        modal_kernel,
        grid=(channels // tile,),
        in_specs=[rows, small, small, small, small, small],
        out_specs=[rows, pl.BlockSpec((modes, tile, 1), lambda i: (0, i, 0))],
        out_shape=[
            jax.ShapeDtypeStruct((channels, length), jnp.float32),
            jax.ShapeDtypeStruct((modes, channels, 1), jnp.float32),
        ],
    )(signal, rate, weight, step, end, span)


def shards(projected, short_weight, skip_weight, decay_rates, residues):
    channels = projected.shape[1]
    length = projected.shape[2]
    feats = short_conv(projected, short_weight)
    mixed = (feats[1] * feats[2]).astype(jnp.bfloat16)
    signal = mixed.astype(jnp.float32)
    weight = residues * jnp.sqrt(2.0 * decay_rates)
    convolved, local_final = local_modal(signal, decay_rates, weight)

    rate = decay_rates.T
    incoming = scan_states(local_final[:, :, 0], rate, length)
    offsets = jnp.arange(1, length + 1, dtype=jnp.float32)
    entering = jnp.sum((weight.T * incoming)[:, :, None] * jnp.exp(-rate[:, :, None] * offsets), axis=0)
    summed = (convolved + entering + skip_weight[:, None] * signal).astype(jnp.bfloat16)
    return (feats[0] * summed.astype(jnp.float32)).astype(jnp.bfloat16)


def solution(mesh):
    return jax.shard_map(
        shards,
        mesh=mesh,
        in_specs=(
            P(None, "fsdp", "seq"),
            P(None, "fsdp", None),
            P("fsdp"),
            P("fsdp", None),
            P("fsdp", None),
        ),
        out_specs=P("fsdp", "seq"),
        check_vma=False,
    )
```

```python
import jax
import jax.numpy as jnp
from jax import lax
from jax.sharding import PartitionSpec as P


def from_behind(value, axis, steps):
    count = lax.axis_size(axis)
    leading, last = (max(0, -steps), min(count, count - steps))
    return lax.ppermute(value, axis, [(source, source + steps) for source in range(leading, last)])


def short_conv(projected, short_weight):
    taps_count = short_weight.shape[2]
    length = projected.shape[2]
    tail = jnp.swapaxes(projected[:, :, length - (taps_count - 1) :], 1, 2)
    before = from_behind(tail, "seq", 1)
    padded = jnp.concatenate([jnp.swapaxes(before, 1, 2), projected], axis=2).astype(jnp.float32)
    feats = jnp.zeros(projected.shape, jnp.float32)
    for lag in range(taps_count):
        begin = taps_count - 1 - lag
        feats = feats + short_weight[:, :, lag][:, :, None] * padded[:, :, begin : begin + length]
    return feats


def scan_states(final, rate, length):
    count = lax.axis_size("seq")

    def earlier(value, steps):
        pairs = [(d, d + steps) for d in range(count) if d + steps < count]
        return lax.ppermute(value, "seq", pairs) if pairs else jnp.zeros_like(value)

    def decay(steps):
        return jnp.exp(-rate * float(length * steps))

    radix = 8
    width = min(radix, count)
    acc = earlier(final, 1)
    for lag in range(2, width + 1):
        acc = acc + decay(lag - 1) * earlier(final, lag)
    while width < count:
        parts = [acc]
        for piece in range(1, radix):
            if piece * width < count:
                parts.append(decay(piece * width) * earlier(acc, piece * width))
        acc = sum(parts[1:], parts[0])
        width *= radix
    return acc


def shards(projected, short_weight, skip_weight, decay_rates, residues):
    channels = projected.shape[1]
    length = projected.shape[2]
    feats = short_conv(projected, short_weight)
    mixed = (feats[1] * feats[2]).astype(jnp.bfloat16)
    signal = mixed.astype(jnp.float32)

    block = min(128, length)
    count = length // block
    rate = decay_rates.T
    weight = (residues * jnp.sqrt(2.0 * decay_rates)).T
    offsets = jnp.arange(block, dtype=jnp.float32)
    rising = jnp.exp(rate[:, :, None] * offsets)
    falling = weight[:, :, None] * jnp.exp(-rate[:, :, None] * offsets)

    blocks = signal.reshape(1, channels, count, block)
    scaled = blocks * rising[:, :, None, :]
    high = scaled.astype(jnp.bfloat16)
    low = (scaled - high.astype(jnp.float32)).astype(jnp.bfloat16)
    rows = jnp.arange(block)
    ones = (rows[:, None] <= rows[None, :]).astype(jnp.bfloat16)
    pair = jnp.concatenate([high, low], axis=3)
    stacked = jnp.concatenate([ones, ones], axis=0)
    running = jnp.einsum("kcni,ij->kcnj", pair, stacked, preferred_element_type=jnp.float32)

    block_sums = jnp.sum(scaled, axis=3) * jnp.exp(-rate * (block - 1))[:, :, None]
    step = jnp.exp(-rate * block)
    carried = [jnp.zeros_like(rate)]
    for n in range(count):
        carried.append(step * carried[-1] + block_sums[:, :, n])
    local_final = carried[-1]
    local_states = jnp.stack(carried[:count], axis=2)

    incoming = scan_states(local_final, rate, length)

    local_part = jnp.exp(-rate)[:, :, None] * local_states
    convolved = jnp.sum(falling[:, :, None, :] * (running + local_part[:, :, :, None]), axis=0)
    starts = (jnp.arange(count) * block + 1).astype(jnp.float32)
    entering = jnp.exp(-rate[:, :, None] * starts) * incoming[:, :, None]
    convolved = convolved + jnp.sum(falling[:, :, None, :] * entering[:, :, :, None], axis=0)
    convolved = convolved.reshape(channels, length)
    summed = (convolved + skip_weight[:, None] * signal).astype(jnp.bfloat16)
    return (feats[0] * summed.astype(jnp.float32)).astype(jnp.bfloat16)


def solution(mesh):
    return jax.shard_map(
        shards,
        mesh=mesh,
        in_specs=(
            P(None, "fsdp", "seq"),
            P(None, "fsdp", None),
            P("fsdp"),
            P("fsdp", None),
            P("fsdp", None),
        ),
        out_specs=P("fsdp", "seq"),
        check_vma=False,
    )
```

```python
import jax
import jax.numpy as jnp
from jax import lax
from jax.sharding import PartitionSpec as P


def from_behind(value, axis, steps):
    count = lax.axis_size(axis)
    leading, last = (max(0, -steps), min(count, count - steps))
    return lax.ppermute(value, axis, [(source, source + steps) for source in range(leading, last)])


def short_conv(projected, short_weight):
    taps_count = short_weight.shape[2]
    length = projected.shape[2]
    tail = jnp.swapaxes(projected[:, :, length - (taps_count - 1) :], 1, 2)
    before = from_behind(tail, "seq", 1)
    padded = jnp.concatenate([jnp.swapaxes(before, 1, 2), projected], axis=2).astype(jnp.float32)
    feats = jnp.zeros(projected.shape, jnp.float32)
    for lag in range(taps_count):
        begin = taps_count - 1 - lag
        feats = feats + short_weight[:, :, lag][:, :, None] * padded[:, :, begin : begin + length]
    return feats


def scan_states(final, rate, length):
    count = lax.axis_size("seq")

    def earlier(value, steps):
        pairs = [(d, d + steps) for d in range(count) if d + steps < count]
        return lax.ppermute(value, "seq", pairs) if pairs else jnp.zeros_like(value)

    def decay(steps):
        return jnp.exp(-rate * float(length * steps))

    width = min(4, count)
    acc = earlier(final, 1)
    for lag in range(2, width + 1):
        acc = acc + decay(lag - 1) * earlier(final, lag)
    while width < count:
        parts = [acc]
        for piece in range(1, 4):
            if piece * width < count:
                parts.append(decay(piece * width) * earlier(acc, piece * width))
        acc = sum(parts[1:], parts[0])
        width *= 4
    return acc


def shards(projected, short_weight, skip_weight, decay_rates, residues):
    channels = projected.shape[1]
    length = projected.shape[2]
    feats = short_conv(projected, short_weight)
    mixed = (feats[1] * feats[2]).astype(jnp.bfloat16)
    signal = mixed.astype(jnp.float32)

    block = min(128, length)
    count = length // block
    rate = decay_rates.T
    weight = (residues * jnp.sqrt(2.0 * decay_rates)).T
    offsets = jnp.arange(block, dtype=jnp.float32)
    rising = jnp.exp(rate[:, :, None] * offsets)
    falling = weight[:, :, None] * jnp.exp(-rate[:, :, None] * offsets)

    blocks = signal.reshape(1, channels, count, block)
    scaled = blocks * rising[:, :, None, :]
    high = scaled.astype(jnp.bfloat16)
    low = (scaled - high.astype(jnp.float32)).astype(jnp.bfloat16)
    rows = jnp.arange(block)
    ones = (rows[:, None] <= rows[None, :]).astype(jnp.bfloat16)
    pair = jnp.concatenate([high, low], axis=3)
    stacked = jnp.concatenate([ones, ones], axis=0)
    running = jnp.einsum("kcni,ij->kcnj", pair, stacked, preferred_element_type=jnp.float32)

    block_sums = jnp.sum(scaled, axis=3) * jnp.exp(-rate * (block - 1))[:, :, None]
    step = jnp.exp(-rate * block)
    carried = [jnp.zeros_like(rate)]
    for n in range(count):
        carried.append(step * carried[-1] + block_sums[:, :, n])
    local_final = carried[-1]
    local_states = jnp.stack(carried[:count], axis=2)

    incoming = scan_states(local_final, rate, length)

    starts = (jnp.arange(count) * block + 1).astype(jnp.float32)
    entering = jnp.exp(-rate)[:, :, None] * local_states + jnp.exp(-rate[:, :, None] * starts) * incoming[:, :, None]
    convolved = jnp.sum(falling[:, :, None, :] * (running + entering[:, :, :, None]), axis=0)
    convolved = convolved.reshape(channels, length)
    summed = (convolved + skip_weight[:, None] * signal).astype(jnp.bfloat16)
    return (feats[0] * summed.astype(jnp.float32)).astype(jnp.bfloat16)


def solution(mesh):
    return jax.shard_map(
        shards,
        mesh=mesh,
        in_specs=(
            P(None, "fsdp", "seq"),
            P(None, "fsdp", None),
            P("fsdp"),
            P("fsdp", None),
            P("fsdp", None),
        ),
        out_specs=P("fsdp", "seq"),
        check_vma=False,
    )
```

```python
import jax
import jax.numpy as jnp
from jax import lax
from jax.sharding import PartitionSpec as P


def from_behind(value, axis, steps):
    count = lax.axis_size(axis)
    leading, last = (max(0, -steps), min(count, count - steps))
    return lax.ppermute(value, axis, [(source, source + steps) for source in range(leading, last)])


def short_conv(projected, short_weight):
    taps_count = short_weight.shape[2]
    length = projected.shape[2]
    tail = jnp.swapaxes(projected[:, :, length - (taps_count - 1) :], 1, 2)
    before = from_behind(tail, "seq", 1)
    padded = jnp.concatenate([jnp.swapaxes(before, 1, 2), projected], axis=2).astype(jnp.float32)
    feats = jnp.zeros(projected.shape, jnp.float32)
    for lag in range(taps_count):
        begin = taps_count - 1 - lag
        feats = feats + short_weight[:, :, lag][:, :, None] * padded[:, :, begin : begin + length]
    return feats


def scan_states(final, rate, length):
    count = lax.axis_size("seq")

    def earlier(value, steps):
        pairs = [(d, d + steps) for d in range(count) if d + steps < count]
        return lax.ppermute(value, "seq", pairs) if pairs else jnp.zeros_like(value)

    def decay(steps):
        return jnp.exp(-rate * float(length * steps))

    width = min(4, count)
    acc = earlier(final, 1)
    for lag in range(2, width + 1):
        acc = acc + decay(lag - 1) * earlier(final, lag)
    while width < count:
        parts = [acc]
        for piece in range(1, 4):
            if piece * width < count:
                parts.append(decay(piece * width) * earlier(acc, piece * width))
        acc = sum(parts[1:], parts[0])
        width *= 4
    return acc


def shards(projected, short_weight, skip_weight, decay_rates, residues):
    channels = projected.shape[1]
    length = projected.shape[2]
    feats = short_conv(projected, short_weight)
    mixed = (feats[1] * feats[2]).astype(jnp.bfloat16)
    signal = mixed.astype(jnp.float32)

    block = min(128, length)
    count = length // block
    rate = decay_rates.T
    weight = (residues * jnp.sqrt(2.0 * decay_rates)).T
    offsets = jnp.arange(block, dtype=jnp.float32)
    rising = jnp.exp(rate[:, :, None] * offsets)
    falling = weight[:, :, None] * jnp.exp(-rate[:, :, None] * offsets)

    modes = rate.shape[0]
    lines = channels * count
    blocks = signal.reshape(1, lines, block)
    spread = lambda table: jnp.broadcast_to(table[:, :, None, :], (modes, channels, count, block)).reshape(
        modes, lines, block
    )
    scaled = blocks * spread(rising)
    high = scaled.astype(jnp.bfloat16)
    low = (scaled - high.astype(jnp.float32)).astype(jnp.bfloat16)
    rows = jnp.arange(block)
    ones = (rows[:, None] <= rows[None, :]).astype(jnp.bfloat16)
    pair = jnp.concatenate([high, low], axis=2)
    stacked = jnp.concatenate([ones, ones], axis=0)
    running = jnp.einsum("kmi,ij->kmj", pair, stacked, preferred_element_type=jnp.float32)

    block_sums = jnp.sum(scaled, axis=2).reshape(modes, channels, count) * jnp.exp(-rate * (block - 1))[:, :, None]
    step = jnp.exp(-rate * block)
    carried = [jnp.zeros_like(rate)]
    for n in range(count):
        carried.append(step * carried[-1] + block_sums[:, :, n])
    local_final = carried[-1]
    local_states = jnp.stack(carried[:count], axis=2)

    incoming = scan_states(local_final, rate, length)

    starts = (jnp.arange(count) * block + 1).astype(jnp.float32)
    entering = jnp.exp(-rate)[:, :, None] * local_states + jnp.exp(-rate[:, :, None] * starts) * incoming[:, :, None]
    convolved = jnp.sum(spread(falling) * (running + entering.reshape(modes, lines, 1)), axis=0)
    convolved = convolved.reshape(channels, length)
    summed = (convolved + skip_weight[:, None] * signal).astype(jnp.bfloat16)
    return (feats[0] * summed.astype(jnp.float32)).astype(jnp.bfloat16)


def solution(mesh):
    return jax.shard_map(
        shards,
        mesh=mesh,
        in_specs=(
            P(None, "fsdp", "seq"),
            P(None, "fsdp", None),
            P("fsdp"),
            P("fsdp", None),
            P("fsdp", None),
        ),
        out_specs=P("fsdp", "seq"),
        check_vma=False,
    )
```

```python
import jax
import jax.numpy as jnp
from jax import lax
from jax.sharding import PartitionSpec as P


def from_behind(value, axis, steps):
    count = lax.axis_size(axis)
    leading, last = (max(0, -steps), min(count, count - steps))
    return lax.ppermute(value, axis, [(source, source + steps) for source in range(leading, last)])


def short_conv(projected, short_weight):
    taps_count = short_weight.shape[2]
    length = projected.shape[2]
    tail = jnp.swapaxes(projected[:, :, length - (taps_count - 1) :], 1, 2)
    before = from_behind(tail, "seq", 1)
    padded = jnp.concatenate([jnp.swapaxes(before, 1, 2), projected], axis=2).astype(jnp.float32)
    feats = jnp.zeros(projected.shape, jnp.float32)
    for lag in range(taps_count):
        begin = taps_count - 1 - lag
        feats = feats + short_weight[:, :, lag][:, :, None] * padded[:, :, begin : begin + length]
    return feats


def scan_states(final, rate, length):
    count = lax.axis_size("seq")

    here = lax.axis_index("seq")

    def earlier(value, steps):
        moved = lax.ppermute(value, "seq", [(d, (d + steps) % count) for d in range(count)])
        return jnp.where(here >= steps, moved, 0.0)

    def decay(steps):
        return jnp.exp(-rate * float(length * steps))

    width = min(4, count)
    acc = earlier(final, 1)
    for lag in range(2, width + 1):
        acc = acc + decay(lag - 1) * earlier(final, lag)
    while width < count:
        parts = [acc]
        for piece in range(1, 4):
            if piece * width < count:
                parts.append(decay(piece * width) * earlier(acc, piece * width))
        acc = sum(parts[1:], parts[0])
        width *= 4
    return acc


def shards(projected, short_weight, skip_weight, decay_rates, residues):
    channels = projected.shape[1]
    length = projected.shape[2]
    feats = short_conv(projected, short_weight)
    mixed = (feats[1] * feats[2]).astype(jnp.bfloat16)
    signal = mixed.astype(jnp.float32)

    block = min(128, length)
    count = length // block
    rate = decay_rates.T
    weight = (residues * jnp.sqrt(2.0 * decay_rates)).T
    offsets = jnp.arange(block, dtype=jnp.float32)
    rising = jnp.exp(rate[:, :, None] * offsets)
    falling = weight[:, :, None] * jnp.exp(-rate[:, :, None] * offsets)

    blocks = signal.reshape(1, channels, count, block)
    scaled = blocks * rising[:, :, None, :]
    high = scaled.astype(jnp.bfloat16)
    low = (scaled - high.astype(jnp.float32)).astype(jnp.bfloat16)
    rows = jnp.arange(block)
    ones = (rows[:, None] <= rows[None, :]).astype(jnp.bfloat16)
    pair = jnp.concatenate([high, low], axis=3)
    stacked = jnp.concatenate([ones, ones], axis=0)
    running = jnp.einsum("kcni,ij->kcnj", pair, stacked, preferred_element_type=jnp.float32)

    block_sums = jnp.sum(scaled, axis=3) * jnp.exp(-rate * (block - 1))[:, :, None]
    step = jnp.exp(-rate * block)
    carried = [jnp.zeros_like(rate)]
    for n in range(count):
        carried.append(step * carried[-1] + block_sums[:, :, n])
    local_final = carried[-1]
    local_states = jnp.stack(carried[:count], axis=2)

    incoming = scan_states(local_final, rate, length)

    starts = (jnp.arange(count) * block + 1).astype(jnp.float32)
    entering = jnp.exp(-rate)[:, :, None] * local_states + jnp.exp(-rate[:, :, None] * starts) * incoming[:, :, None]
    convolved = jnp.sum(falling[:, :, None, :] * (running + entering[:, :, :, None]), axis=0)
    convolved = convolved.reshape(channels, length)
    summed = (convolved + skip_weight[:, None] * signal).astype(jnp.bfloat16)
    return (feats[0] * summed.astype(jnp.float32)).astype(jnp.bfloat16)


def solution(mesh):
    return jax.shard_map(
        shards,
        mesh=mesh,
        in_specs=(
            P(None, "fsdp", "seq"),
            P(None, "fsdp", None),
            P("fsdp"),
            P("fsdp", None),
            P("fsdp", None),
        ),
        out_specs=P("fsdp", "seq"),
        check_vma=False,
    )
```
